128 devices in a mesh: sec: 2 (over x_hi), head: 4 (over x_lo, core), ctx: 16 (over z, y).
Axes of the slice: x: 4 (x_hi: 2, x_lo: 2; x = x_hi * 2 + x_lo), y: 4, z: 4, core: 2. Of those that a mesh axis runs over, the one named last changes fastest.
Arguments:
- proposal_rows: bfloat16 [512, 8192], P('sec', 'ctx'), may hold values from -400 to 400
- norm_gain: bfloat16 [8192], P('ctx'), may hold values from 0.25 to 1.75
- query_weight: bfloat16 [8192, 8192], P('ctx', ('sec', 'head')), may hold values from -0.0625 to 0.0625
- key_weight: bfloat16 [8192, 8, 128], P('ctx', ('sec', 'head')), may hold values from -0.25 to 0.25
- value_weight: bfloat16 [8192, 8, 128], P('ctx', ('sec', 'head')), may hold values from -0.0625 to 0.0625
- out_weight: bfloat16 [8192, 8192], P(('sec', 'head'), 'ctx'), may hold values from -0.0625 to 0.0625
- context_keys: bfloat16 [32768, 8, 128], P('ctx', ('sec', 'head')), may hold values from -256 to 256
- context_values: bfloat16 [32768, 8, 128], P('ctx', ('sec', 'head')), may hold values from -5 to 5
- prefix_lengths: int32 [32], replicated, may hold values from 2048 to 32768, as said below
- parents: int32 [512], replicated, may hold values from -1 to 510, as said below
Outputs:
- block_output: bfloat16 [512, 8192], P(('sec', 'head'), 'ctx')
The draws below stay inside these ranges and needn't reach their ends.
Inputs may be any that keep to these rules, and one draw needn't show every extreme that they name: `parents`: token i = 16 p + s of particle p has parent -1 when s = 0, else 16 q + s - 1 for some particle q <= p. `prefix_lengths`: some particle sees the whole context.
All inputs are finite; a program needn't handle non-finite values.
Results may differ from the reference program's by a relative error of at most 0.015.
The reference program's roundings to bfloat16 on the way count: a program that leaves them out, or rounds other values in their place, can miss the bound.
Values may be sent and summed in bfloat16 or wider, within the bound.
No kernel may reach another device: no remote copies, remote signals or barrier semaphores. Data moves between devices by JAX's collectives and lax.ppermute only.
A program may use at most 192 MiB of HBM per device.

```python
import math
import jax
import jax.numpy as jnp
from jax import lax

D = 8192
HEADS = 64
KVH = 8
HD = 128
PARTICLES = 32
PROPOSALS = 16
CTX_DEV = 2048
TREE = 512
CTX = 32768
GROUP = 8
N_CTX = 16


def draw_proposal_rows(key, part):
    earlier, later, column_key = jax.random.split(key, 3)
    ramp = jnp.arange(D, dtype=jnp.float32) / D
    column_scale = 0.3 * jnp.exp(math.log(3.0) * ramp) * jnp.exp(jax.random.uniform(column_key, (D,), jnp.float32, 0.0, math.log(10.0)))
    noise = jax.random.truncated_normal(earlier, -4.0, 4.0, (TREE, D), jnp.float32)
    row_scale = jnp.exp(jax.random.uniform(later, (TREE, 1), jnp.float32, 0.0, math.log(10.0)))
    return (noise * row_scale * column_scale[None, :]).astype(jnp.bfloat16)


def draw_context_keys(key, part):
    earlier = jax.random.fold_in(key, 0)
    noise = jax.random.truncated_normal(earlier, -4.5, 4.5, (CTX, KVH, HD), jnp.float32)
    return noise.astype(jnp.bfloat16)


def draw_prefix_lengths(key, part):
    earlier, later = jax.random.split(key)
    lowest = max(CTX // 16, 1)
    values = jax.random.randint(earlier, (PARTICLES,), lowest, CTX + 1, dtype=jnp.int32)
    chosen = jax.random.randint(later, (), 0, PARTICLES, dtype=jnp.int32)
    return jnp.where(jnp.arange(PARTICLES, dtype=jnp.int32) == chosen, CTX, values).astype(jnp.int32)


def draw_parents(key, part):
    position = jnp.arange(TREE, dtype=jnp.int32)
    particle = position // PROPOSALS
    depth_index = position % PROPOSALS
    jump_draw = jax.random.randint(key, (TREE,), 0, 8, dtype=jnp.int32)
    source = jnp.where(jump_draw < 4, jnp.maximum(particle - 1 - jump_draw, 0), particle)
    source = jnp.where(particle == PARTICLES - 1, particle, source)
    return jnp.where(depth_index == 0, -1, source * PROPOSALS + depth_index - 1).astype(jnp.int32)


def block_scale(own_key, extent, cuts, least, high):
    def one(axis_at, shards_of):
        heights = jax.random.uniform(jax.random.fold_in(jax.random.fold_in(own_key, 6), axis_at), (shards_of,), jnp.float32, least / len(cuts), high / len(cuts))
        return jnp.repeat(jnp.exp(heights), extent[axis_at] // shards_of).reshape((-1,) + (1,) * (len(extent) - axis_at - 1))

    gain = one(*cuts[0])
    for cut in cuts[1:]:
        gain = gain * one(*cut)
    return gain


def scatter_about(rng, dims, scale, bound, shards=(), kind=jnp.bfloat16):
    gain = block_scale(rng, dims, shards, -0.22, 0.18) if shards else 1.0
    entries = jax.random.normal(rng, dims, jnp.float32) * scale * gain
    return jnp.minimum(jnp.maximum(entries, -bound), bound).astype(kind)


def setup_inputs(seed: int = 0) -> dict:
    arg_keys = jax.random.split(jax.random.key(seed), 11)
    return {
        "proposal_rows": draw_proposal_rows(jax.random.fold_in(arg_keys[10], 71), 0),
        "norm_gain": jnp.clip(1.0 + 0.15 * jax.random.normal(arg_keys[1], (D,), jnp.float32), 0.25, 1.75).astype(jnp.bfloat16),
        "query_weight": scatter_about(arg_keys[2], (D, HEADS * HD), D ** -0.5, 0.0625, ((0, 16), (1, 8))),
        "key_weight": scatter_about(arg_keys[3], (D, KVH, HD), (D // 16) ** -0.5, 0.25, ((0, 16), (1, 8))),
        "value_weight": scatter_about(arg_keys[4], (D, KVH, HD), D ** -0.5, 0.0625, ((0, 16), (1, 8))),
        "out_weight": scatter_about(arg_keys[5], (HEADS * HD, D), (HEADS * HD) ** -0.5, 0.0625, ((0, 8), (1, 16))),
        "context_keys": draw_context_keys(jax.random.fold_in(arg_keys[10], 71), 0),
        "context_values": scatter_about(arg_keys[7], (CTX, KVH, HD), 1.0, 5.0, ((0, 16), (1, 8))),
        "prefix_lengths": draw_prefix_lengths(jax.random.fold_in(arg_keys[10], 71), 0),
        "parents": draw_parents(jax.random.fold_in(arg_keys[10], 71), 0),
    }


NEGATIVE = -1e+30
EPSILON = 1e-05

def ancestry(parents, query_rows, key_offset, key_amount):
    key_index = key_offset + jnp.arange(key_amount, dtype=jnp.int32)

    def advance(turn_index, carried):
        current, reached = carried
        reached = jnp.logical_or(reached, current[:, None] == key_index[None, :])
        upward = jnp.take(parents, jnp.maximum(current, 0))
        return (jnp.where(current >= 0, upward, -1).astype(jnp.int32), reached)
    initial = (query_rows.astype(jnp.int32), jnp.zeros((query_rows.shape[0], key_amount), dtype=bool))
    return lax.fori_loop(0, PROPOSALS, advance, initial)[1]

def absorb(carried, scores, visible, values):
    summed, highest, weight_sum = carried
    newest = jnp.maximum(highest, lax.optimization_barrier(jnp.max(jnp.where(visible, scores, NEGATIVE), axis=2)))
    weights = jnp.where(visible, jnp.exp(scores - newest[:, :, None]), 0.0)
    shrink = jnp.exp(highest - newest)
    rounded = lax.optimization_barrier(weights.astype(jnp.bfloat16))
    weight_sum = weight_sum * shrink + lax.optimization_barrier(jnp.sum(weights, axis=2))
    summed = summed * shrink[:, :, None] + jnp.einsum('rgt,td->rgd', rounded.astype(jnp.float32), values.astype(jnp.float32))
    return (summed, newest, weight_sum)

def reference(proposal_rows, norm_gain, query_weight, key_weight, value_weight, out_weight, context_keys, context_values, prefix_lengths, parents):
    rows_wide = proposal_rows.astype(jnp.float32)
    squares = lax.optimization_barrier(jnp.sum(rows_wide * rows_wide, axis=1))
    inverse = lax.rsqrt(squares / D + EPSILON)[:, None]
    scaled = (rows_wide * norm_gain.astype(jnp.float32)[None, :]).astype(jnp.bfloat16)
    queries = (jnp.dot(scaled, query_weight, preferred_element_type=jnp.float32) * inverse).astype(jnp.bfloat16)
    tree_keys = (jnp.dot(scaled, key_weight.reshape(D, KVH * HD), preferred_element_type=jnp.float32) * inverse).astype(jnp.bfloat16).reshape(TREE, KVH, HD)
    tree_values = (jnp.dot(scaled, value_weight.reshape(D, KVH * HD), preferred_element_type=jnp.float32) * inverse).astype(jnp.bfloat16).reshape(TREE, KVH, HD)
    lengths_rows = jnp.repeat(prefix_lengths, PROPOSALS)
    visible_tree = ancestry(parents, jnp.arange(TREE, dtype=jnp.int32), 0, TREE)
    factor = 1.0 / math.sqrt(HD)

    def per_head(kv_index):
        grouped = lax.dynamic_slice_in_dim(queries, kv_index * (GROUP * HD), GROUP * HD, 1).astype(jnp.float32).reshape(TREE, GROUP, HD)
        key_blocks = lax.dynamic_index_in_dim(context_keys, kv_index, 1, keepdims=False).reshape(N_CTX, CTX_DEV, HD)
        value_blocks = lax.dynamic_index_in_dim(context_values, kv_index, 1, keepdims=False).reshape(N_CTX, CTX_DEV, HD)

        def scan_block(carried, pieces):
            block_keys, block_values, block_offset = pieces
            scores = jnp.einsum('rgd,td->rgt', grouped, block_keys.astype(jnp.float32)) * factor
            positions = block_offset + jnp.arange(CTX_DEV, dtype=jnp.int32)
            visible = (positions[None, :] < lengths_rows[:, None])[:, None, :]
            return (absorb(carried, scores, visible, block_values), None)
        initial = (jnp.zeros((TREE, GROUP, HD), jnp.float32), jnp.full((TREE, GROUP), NEGATIVE, jnp.float32), jnp.zeros((TREE, GROUP), jnp.float32))
        offsets = jnp.arange(N_CTX, dtype=jnp.int32) * CTX_DEV
        carried, _ = lax.scan(scan_block, initial, (key_blocks, value_blocks, offsets))
        head_keys = lax.dynamic_index_in_dim(tree_keys, kv_index, 1, keepdims=False)
        head_values = lax.dynamic_index_in_dim(tree_values, kv_index, 1, keepdims=False)
        scores = jnp.einsum('rgd,td->rgt', grouped, head_keys.astype(jnp.float32)) * factor
        summed, highest, weight_sum = absorb(carried, scores, visible_tree[:, None, :], head_values)
        return (summed / weight_sum[:, :, None]).reshape(TREE, GROUP * HD)
    heads_out = lax.map(per_head, jnp.arange(KVH, dtype=jnp.int32))
    attended = jnp.transpose(heads_out, (1, 0, 2)).reshape(TREE, HEADS * HD).astype(jnp.bfloat16)
    return jnp.dot(attended, out_weight, preferred_element_type=jnp.float32).astype(jnp.bfloat16)
```

```python
import math

import jax
import jax.numpy as jnp
from jax import lax
from jax.sharding import PartitionSpec as P

D = 8192
PROPOSALS = 16


NEGATIVE = -1e30
EPSILON = 1e-05


def ancestry_columns(parents, column_offset, column_amount):
    total = parents.shape[0]
    index = jnp.arange(total, dtype=jnp.int32)
    step = jnp.logical_or(parents[:, None] == index[None, :], index[:, None] == index[None, :])
    reach = step.astype(jnp.bfloat16)
    for _ in range(3):
        reach = (jnp.dot(reach, reach, preferred_element_type=jnp.float32) > 0).astype(jnp.bfloat16)
    columns = lax.dynamic_slice_in_dim(reach, column_offset, column_amount, 1)
    return jnp.dot(reach, columns, preferred_element_type=jnp.float32) > 0


def body(
    proposal_rows,
    norm_gain,
    query_weight,
    key_weight,
    value_weight,
    out_weight,
    context_keys,
    context_values,
    prefix_lengths,
    parents,
):
    gathered = lax.all_gather(proposal_rows, "sec", axis=0, tiled=True)
    gathered_wide = gathered.astype(jnp.float32)
    total_rows = gathered.shape[0]
    squares = jnp.sum(gathered_wide * gathered_wide, axis=1)
    scaled = (gathered_wide * norm_gain.astype(jnp.float32)[None, :]).astype(jnp.bfloat16)
    query_width = query_weight.shape[1]
    head_size = key_weight.shape[2]
    groups = query_width // head_size
    joined = jnp.concatenate([query_weight, key_weight[:, 0, :], value_weight[:, 0, :]], axis=1)
    partial_value = jnp.dot(scaled, joined, preferred_element_type=jnp.float32)
    proj_width = partial_value.shape[1]
    lane = jnp.arange(128, dtype=jnp.int32)
    square_block = jnp.where(lane[None, :] == 0, squares[:, None], 0.0)
    packed = jnp.concatenate([partial_value, square_block], axis=1)
    reduced = lax.psum_scatter(packed, "ctx", scatter_dimension=0, tiled=True)
    row_share = reduced.shape[0]
    inverse = lax.rsqrt(reduced[:, proj_width] / D + EPSILON)[:, None]
    settled = reduced[:, :proj_width] * inverse
    own_queries = settled[:, :query_width].astype(jnp.bfloat16)
    tree_keys = settled[:, query_width : query_width + head_size].astype(jnp.bfloat16)
    tree_vals = settled[:, query_width + head_size :].astype(jnp.bfloat16)
    queries = lax.all_gather(own_queries, "ctx", axis=0, tiled=True)

    position = lax.axis_index("ctx")
    keys = context_keys[:, 0, :]
    vals = context_values[:, 0, :]
    span = keys.shape[0]
    factor = 1.0 / math.sqrt(head_size)
    grouped = queries.reshape(total_rows, groups, head_size)
    lengths_rows = jnp.repeat(prefix_lengths, PROPOSALS)
    positions = position * span + jnp.arange(span, dtype=jnp.int32)
    visible = (positions[None, :] < lengths_rows[:, None])[:, None, :]
    scores = jnp.einsum("rgd,td->rgt", grouped, keys, preferred_element_type=jnp.float32) * factor
    tree_visible = ancestry_columns(parents, position * row_share, row_share)[:, None, :]
    tree_scores = (
        jnp.einsum("rgd,td->rgt", grouped, tree_keys, preferred_element_type=jnp.float32) * factor
    )
    local_high = jnp.maximum(
        jnp.max(jnp.where(visible, scores, NEGATIVE), axis=2),
        jnp.max(jnp.where(tree_visible, tree_scores, NEGATIVE), axis=2),
    )
    highest = lax.pmax(local_high, "ctx")
    weights = jnp.where(visible, jnp.exp(scores - highest[:, :, None]), 0.0)
    tree_weights = jnp.where(tree_visible, jnp.exp(tree_scores - highest[:, :, None]), 0.0)
    weight_sum = jnp.sum(weights, axis=2) + jnp.sum(tree_weights, axis=2)
    summed = jnp.einsum(
        "rgt,td->rgd", weights.astype(jnp.bfloat16), vals, preferred_element_type=jnp.float32
    ) + jnp.einsum(
        "rgt,td->rgd", tree_weights.astype(jnp.bfloat16), tree_vals, preferred_element_type=jnp.float32
    )
    sum_block = jnp.concatenate(
        [weight_sum, jnp.zeros((total_rows, 128 - groups), jnp.float32)], axis=1
    )
    packed_attn = jnp.concatenate([summed.reshape(total_rows, query_width), sum_block], axis=1)
    merged = lax.psum_scatter(packed_attn, "ctx", scatter_dimension=0, tiled=True)
    own_attended = (
        (merged[:, :query_width].reshape(row_share, groups, head_size)
         / merged[:, query_width : query_width + groups][:, :, None])
        .reshape(row_share, query_width)
        .astype(jnp.bfloat16)
    )
    attended = lax.all_gather(own_attended, "ctx", axis=0, tiled=True)
    return lax.psum_scatter(
        jnp.dot(attended, out_weight, preferred_element_type=jnp.float32).astype(jnp.bfloat16),
        ("sec", "head"),
        scatter_dimension=0,
        tiled=True,
    )


def solution(mesh):
    placed = (
        P("sec", "ctx"),
        P("ctx"),
        P("ctx", ("sec", "head")),
        P("ctx", ("sec", "head"), None),
        P("ctx", ("sec", "head"), None),
        P(("sec", "head"), "ctx"),
        P("ctx", ("sec", "head"), None),
        P("ctx", ("sec", "head"), None),
        P(),
        P(),
    )
    return jax.shard_map(
        body, mesh=mesh, in_specs=placed, out_specs=P(("sec", "head"), "ctx"), check_vma=False
    )
```

```python
import math

import jax
import jax.numpy as jnp
from jax import lax
from jax.sharding import PartitionSpec as P

D = 8192
PROPOSALS = 16


NEGATIVE = -1e30
EPSILON = 1e-05


def ancestry_columns(parents, column_offset, column_amount):
    total = parents.shape[0]
    index = jnp.arange(total, dtype=jnp.int32)
    step = jnp.logical_or(parents[:, None] == index[None, :], index[:, None] == index[None, :])
    reach = step.astype(jnp.bfloat16)
    for _ in range(3):
        reach = (jnp.dot(reach, reach, preferred_element_type=jnp.float32) > 0).astype(jnp.bfloat16)
    columns = lax.dynamic_slice_in_dim(reach, column_offset, column_amount, 1)
    return jnp.dot(reach, columns, preferred_element_type=jnp.float32) > 0


def reduce_rows(value, axis):
    count = lax.axis_size(axis)
    moved = lax.all_to_all(value, axis, 0, 0, tiled=True)
    return jnp.sum(moved.reshape(count, -1, *value.shape[1:]), axis=0)


def gather_rows(value, axis):
    count = lax.axis_size(axis)
    return lax.all_to_all(jnp.tile(value, (count, 1)), axis, 0, 0, tiled=True)


def body(
    proposal_rows,
    norm_gain,
    query_weight,
    key_weight,
    value_weight,
    out_weight,
    context_keys,
    context_values,
    prefix_lengths,
    parents,
):
    other_rows = lax.ppermute(proposal_rows, "sec", [(0, 1), (1, 0)])
    first = lax.axis_index("sec") == 0
    gathered = jnp.where(
        first,
        jnp.concatenate([proposal_rows, other_rows], axis=0),
        jnp.concatenate([other_rows, proposal_rows], axis=0),
    )
    gathered_wide = gathered.astype(jnp.float32)
    total_rows = gathered.shape[0]
    squares = jnp.sum(gathered_wide * gathered_wide, axis=1)
    scaled = (gathered_wide * norm_gain.astype(jnp.float32)[None, :]).astype(jnp.bfloat16)
    query_width = query_weight.shape[1]
    head_size = key_weight.shape[2]
    groups = query_width // head_size
    joined = jnp.concatenate([query_weight, key_weight[:, 0, :], value_weight[:, 0, :]], axis=1)
    partial_value = jnp.dot(scaled, joined, preferred_element_type=jnp.float32)
    proj_width = partial_value.shape[1]
    lane = jnp.arange(128, dtype=jnp.int32)
    square_block = jnp.where(lane[None, :] == 0, squares[:, None], 0.0)
    packed = jnp.concatenate([partial_value, square_block], axis=1)
    reduced = reduce_rows(packed, "ctx")
    row_share = reduced.shape[0]
    inverse = lax.rsqrt(reduced[:, proj_width] / D + EPSILON)[:, None]
    settled = reduced[:, :proj_width] * inverse
    own_queries = settled[:, :query_width].astype(jnp.bfloat16)
    tree_keys = settled[:, query_width : query_width + head_size].astype(jnp.bfloat16)
    tree_vals = settled[:, query_width + head_size :].astype(jnp.bfloat16)
    queries = gather_rows(own_queries, "ctx")

    position = lax.axis_index("ctx")
    keys = context_keys[:, 0, :]
    vals = context_values[:, 0, :]
    span = keys.shape[0]
    factor = 1.0 / math.sqrt(head_size)
    grouped = queries.reshape(total_rows, groups, head_size)
    lengths_rows = jnp.repeat(prefix_lengths, PROPOSALS)
    positions = position * span + jnp.arange(span, dtype=jnp.int32)
    visible = (positions[None, :] < lengths_rows[:, None])[:, None, :]
    scores = jnp.einsum("rgd,td->rgt", grouped, keys, preferred_element_type=jnp.float32) * factor
    tree_visible = ancestry_columns(parents, position * row_share, row_share)[:, None, :]
    tree_scores = (
        jnp.einsum("rgd,td->rgt", grouped, tree_keys, preferred_element_type=jnp.float32) * factor
    )
    local_high = jnp.maximum(
        jnp.max(jnp.where(visible, scores, NEGATIVE), axis=2),
        jnp.max(jnp.where(tree_visible, tree_scores, NEGATIVE), axis=2),
    )
    weights = jnp.where(visible, jnp.exp(scores - local_high[:, :, None]), 0.0)
    tree_weights = jnp.where(tree_visible, jnp.exp(tree_scores - local_high[:, :, None]), 0.0)
    weight_sum = jnp.sum(weights, axis=2) + jnp.sum(tree_weights, axis=2)
    summed = jnp.einsum(
        "rgt,td->rgd", weights.astype(jnp.bfloat16), vals, preferred_element_type=jnp.float32
    ) + jnp.einsum(
        "rgt,td->rgd", tree_weights.astype(jnp.bfloat16), tree_vals, preferred_element_type=jnp.float32
    )
    side_block = jnp.concatenate(
        [weight_sum, local_high, jnp.zeros((total_rows, 128 - 2 * groups), jnp.float32)], axis=1
    )
    packed_attn = jnp.concatenate([summed.reshape(total_rows, query_width), side_block], axis=1)
    count = lax.axis_size("ctx")
    moved = lax.all_to_all(packed_attn, "ctx", 0, 0, tiled=True).reshape(count, row_share, -1)
    shard_sums = moved[:, :, :query_width].reshape(count, row_share, groups, head_size)
    shard_weights = moved[:, :, query_width : query_width + groups]
    shard_high = moved[:, :, query_width + groups : query_width + 2 * groups]
    top = jnp.max(shard_high, axis=0)
    shrink = jnp.exp(shard_high - top[None])
    total_sums = jnp.sum(shard_sums * shrink[:, :, :, None], axis=0)
    total_weights = jnp.sum(shard_weights * shrink, axis=0)
    own_attended = (
        (total_sums / total_weights[:, :, None]).reshape(row_share, query_width).astype(jnp.bfloat16)
    )
    attended = gather_rows(own_attended, "ctx")
    projected_out = jnp.dot(attended, out_weight, preferred_element_type=jnp.float32)
    return reduce_rows(projected_out, ("sec", "head")).astype(jnp.bfloat16)


def solution(mesh):
    placed = (
        P("sec", "ctx"),
        P("ctx"),
        P("ctx", ("sec", "head")),
        P("ctx", ("sec", "head"), None),
        P("ctx", ("sec", "head"), None),
        P(("sec", "head"), "ctx"),
        P("ctx", ("sec", "head"), None),
        P("ctx", ("sec", "head"), None),
        P(),
        P(),
    )
    return jax.shard_map(
        body, mesh=mesh, in_specs=placed, out_specs=P(("sec", "head"), "ctx"), check_vma=False
    )
```

```python
import math

import jax
import jax.numpy as jnp
from jax import lax
from jax.sharding import PartitionSpec as P

D = 8192
PROPOSALS = 16


NEGATIVE = -1e30
EPSILON = 1e-05


def ancestry_columns(parents, column_offset, column_amount):
    total = parents.shape[0]
    index = jnp.arange(total, dtype=jnp.int32)
    step = jnp.logical_or(parents[:, None] == index[None, :], index[:, None] == index[None, :])
    reach = step.astype(jnp.bfloat16)
    for _ in range(3):
        reach = (jnp.dot(reach, reach, preferred_element_type=jnp.float32) > 0).astype(jnp.bfloat16)
    columns = lax.dynamic_slice_in_dim(reach, column_offset, column_amount, 1)
    return jnp.dot(reach, columns, preferred_element_type=jnp.float32) > 0


def reduce_rows(value, axis):
    count = lax.axis_size(axis)
    moved = lax.all_to_all(value, axis, 0, 0, tiled=True)
    return jnp.sum(moved.reshape(count, -1, *value.shape[1:]), axis=0)


def gather_rows(value, axis):
    count = lax.axis_size(axis)
    return lax.all_to_all(jnp.tile(value, (count, 1)), axis, 0, 0, tiled=True)


def body(
    proposal_rows,
    norm_gain,
    query_weight,
    key_weight,
    value_weight,
    out_weight,
    context_keys,
    context_values,
    prefix_lengths,
    parents,
):
    other_rows = lax.ppermute(proposal_rows, "sec", [(0, 1), (1, 0)])
    first = lax.axis_index("sec") == 0
    gathered = jnp.where(
        first,
        jnp.concatenate([proposal_rows, other_rows], axis=0),
        jnp.concatenate([other_rows, proposal_rows], axis=0),
    )
    gathered_wide = gathered.astype(jnp.float32)
    total_rows = gathered.shape[0]
    squares = jnp.sum(gathered_wide * gathered_wide, axis=1)
    scaled = (gathered_wide * norm_gain.astype(jnp.float32)[None, :]).astype(jnp.bfloat16)
    query_width = query_weight.shape[1]
    head_size = key_weight.shape[2]
    groups = query_width // head_size
    joined = jnp.concatenate([query_weight, key_weight[:, 0, :], value_weight[:, 0, :]], axis=1)
    partial_value = jnp.dot(scaled, joined, preferred_element_type=jnp.float32)
    proj_width = partial_value.shape[1]
    lane = jnp.arange(128, dtype=jnp.int32)
    square_block = jnp.where(lane[None, :] == 0, squares[:, None], 0.0)
    packed = jnp.concatenate([partial_value, square_block], axis=1)
    reduced = reduce_rows(packed, "ctx")
    row_share = reduced.shape[0]
    inverse = lax.rsqrt(reduced[:, proj_width] / D + EPSILON)[:, None]
    settled = reduced[:, :proj_width] * inverse
    own_queries = settled[:, :query_width].astype(jnp.bfloat16)
    tree_keys = settled[:, query_width : query_width + head_size].astype(jnp.bfloat16)
    tree_vals = settled[:, query_width + head_size :].astype(jnp.bfloat16)
    queries = gather_rows(own_queries, "ctx")

    position = lax.axis_index("ctx")
    keys = context_keys[:, 0, :]
    vals = context_values[:, 0, :]
    span = keys.shape[0]
    factor = 1.0 / math.sqrt(head_size)
    grouped = queries.reshape(total_rows, groups, head_size)
    lengths_rows = jnp.repeat(prefix_lengths, PROPOSALS)
    positions = position * span + jnp.arange(span, dtype=jnp.int32)
    visible = (positions[None, :] < lengths_rows[:, None])[:, None, :]
    scores = jnp.einsum("rgd,td->rgt", grouped, keys, preferred_element_type=jnp.float32) * factor
    tree_visible = ancestry_columns(parents, position * row_share, row_share)[:, None, :]
    tree_scores = (
        jnp.einsum("rgd,td->rgt", grouped, tree_keys, preferred_element_type=jnp.float32) * factor
    )
    local_high = jnp.maximum(
        jnp.max(jnp.where(visible, scores, NEGATIVE), axis=2),
        jnp.max(jnp.where(tree_visible, tree_scores, NEGATIVE), axis=2),
    )
    high_hi = lax.reduce_precision(local_high, exponent_bits=8, mantissa_bits=7)
    high_lo = lax.reduce_precision(local_high - high_hi, exponent_bits=8, mantissa_bits=7)
    local_high = high_hi + high_lo
    weights = jnp.where(visible, jnp.exp(scores - local_high[:, :, None]), 0.0)
    tree_weights = jnp.where(tree_visible, jnp.exp(tree_scores - local_high[:, :, None]), 0.0)
    weight_sum = jnp.sum(weights, axis=2) + jnp.sum(tree_weights, axis=2)
    summed = jnp.einsum(
        "rgt,td->rgd", weights.astype(jnp.bfloat16), vals, preferred_element_type=jnp.float32
    ) + jnp.einsum(
        "rgt,td->rgd", tree_weights.astype(jnp.bfloat16), tree_vals, preferred_element_type=jnp.float32
    )
    sum_hi = lax.reduce_precision(weight_sum, exponent_bits=8, mantissa_bits=7)
    sum_lo = weight_sum - sum_hi
    side_block = jnp.concatenate(
        [sum_hi, sum_lo, high_hi, high_lo, jnp.zeros((total_rows, 128 - 4 * groups), jnp.float32)],
        axis=1,
    ).astype(jnp.bfloat16)
    packed_attn = jnp.concatenate(
        [summed.reshape(total_rows, query_width).astype(jnp.bfloat16), side_block], axis=1
    )
    count = lax.axis_size("ctx")
    moved = lax.all_to_all(packed_attn, "ctx", 0, 0, tiled=True).reshape(count, row_share, -1)
    moved = moved.astype(jnp.float32)
    shard_sums = moved[:, :, :query_width].reshape(count, row_share, groups, head_size)
    side = moved[:, :, query_width : query_width + 4 * groups].reshape(count, row_share, 4, groups)
    shard_weights = side[:, :, 0] + side[:, :, 1]
    shard_high = side[:, :, 2] + side[:, :, 3]
    top = jnp.max(shard_high, axis=0)
    shrink = jnp.exp(shard_high - top[None])
    total_sums = jnp.sum(shard_sums * shrink[:, :, :, None], axis=0)
    total_weights = jnp.sum(shard_weights * shrink, axis=0)
    own_attended = (
        (total_sums / total_weights[:, :, None]).reshape(row_share, query_width).astype(jnp.bfloat16)
    )
    attended = gather_rows(own_attended, "ctx")
    projected_out = jnp.dot(attended, out_weight, preferred_element_type=jnp.float32)
    return reduce_rows(projected_out, ("sec", "head")).astype(jnp.bfloat16)


def solution(mesh):
    placed = (
        P("sec", "ctx"),
        P("ctx"),
        P("ctx", ("sec", "head")),
        P("ctx", ("sec", "head"), None),
        P("ctx", ("sec", "head"), None),
        P(("sec", "head"), "ctx"),
        P("ctx", ("sec", "head"), None),
        P("ctx", ("sec", "head"), None),
        P(),
        P(),
    )
    return jax.shard_map(
        body, mesh=mesh, in_specs=placed, out_specs=P(("sec", "head"), "ctx"), check_vma=False
    )
```

```python
import math

import jax
import jax.numpy as jnp
from jax import lax
from jax.experimental import pallas as pl
from jax.experimental.pallas import tpu as pltpu
from jax.sharding import PartitionSpec as P

D = 8192
PROPOSALS = 16


NEGATIVE = -1e30
EPSILON = 1e-05


def ancestry_columns(parents, column_offset, column_amount):
    total = parents.shape[0]
    index = jnp.arange(total, dtype=jnp.int32)
    step = jnp.logical_or(parents[:, None] == index[None, :], index[:, None] == index[None, :])
    reach = step.astype(jnp.bfloat16)
    for _ in range(3):
        reach = (jnp.dot(reach, reach, preferred_element_type=jnp.float32) > 0).astype(jnp.bfloat16)
    columns = lax.dynamic_slice_in_dim(reach, column_offset, column_amount, 1)
    return jnp.dot(reach, columns, preferred_element_type=jnp.float32) > 0


def split_three(value):
    high = lax.reduce_precision(value, exponent_bits=8, mantissa_bits=7)
    rest = value - high
    middle = lax.reduce_precision(rest, exponent_bits=8, mantissa_bits=7)
    return high, middle, rest - middle


def attend_kernel(
    query_ref, key_ref, value_ref, length_ref, tree_key_ref, tree_value_ref, tree_mask_ref,
    out_ref, high_ref, total_ref, *, factor,
):
    query = query_ref[...]
    scores = lax.dot_general(
        query, key_ref[...], (((1,), (1,)), ((), ())), preferred_element_type=jnp.float32
    ) * factor
    place = lax.broadcasted_iota(jnp.int32, scores.shape, 1)
    visible = place < length_ref[...]
    scores = jnp.where(visible, scores, NEGATIVE)
    tree_scores = lax.dot_general(
        query, tree_key_ref[...], (((1,), (1,)), ((), ())), preferred_element_type=jnp.float32
    ) * factor
    tree_visible = tree_mask_ref[...] > 0
    tree_scores = jnp.where(tree_visible, tree_scores, NEGATIVE)
    high = jnp.maximum(
        jnp.max(scores, axis=1, keepdims=True), jnp.max(tree_scores, axis=1, keepdims=True)
    )
    weights = jnp.where(visible, jnp.exp(scores - high), 0.0)
    tree_weights = jnp.where(tree_visible, jnp.exp(tree_scores - high), 0.0)
    total_ref[...] = jnp.sum(weights, axis=1, keepdims=True) + jnp.sum(
        tree_weights, axis=1, keepdims=True
    )
    high_ref[...] = high
    out_ref[...] = (
        jnp.dot(weights.astype(jnp.bfloat16), value_ref[...], preferred_element_type=jnp.float32)
        + jnp.dot(
            tree_weights.astype(jnp.bfloat16), tree_value_ref[...],
            preferred_element_type=jnp.float32,
        )
    ).astype(jnp.bfloat16)


def attend(query, keys, vals, lengths, tree_keys, tree_vals, tree_mask, factor, block=512):
    amount, head_size = query.shape
    span = keys.shape[0]
    tree_amount = tree_keys.shape[0]
    whole = lambda i: (0, 0)
    rows = lambda i: (i, 0)
    return pl.pallas_call(
        lambda *refs: attend_kernel(*refs, factor=factor),
        out_shape=(
            jax.ShapeDtypeStruct((amount, head_size), jnp.bfloat16),
            jax.ShapeDtypeStruct((amount, 1), jnp.float32),
            jax.ShapeDtypeStruct((amount, 1), jnp.float32),
        ),
        grid=(amount // block,),
        in_specs=[
            pl.BlockSpec((block, head_size), rows),
            pl.BlockSpec((span, head_size), whole),
            pl.BlockSpec((span, head_size), whole),
            pl.BlockSpec((block, 1), rows),
            pl.BlockSpec((tree_amount, head_size), whole),
            pl.BlockSpec((tree_amount, head_size), whole),
            pl.BlockSpec((block, tree_amount), rows),
        ],
        out_specs=(
            pl.BlockSpec((block, head_size), rows),
            pl.BlockSpec((block, 1), rows),
            pl.BlockSpec((block, 1), rows),
        ),
        compiler_params=pltpu.CompilerParams(dimension_semantics=("arbitrary",)),
    )(query, keys, vals, lengths, tree_keys, tree_vals, tree_mask)


def reduce_rows(value, axis):
    count = lax.axis_size(axis)
    moved = lax.all_to_all(value, axis, 0, 0, tiled=True)
    return jnp.sum(moved.reshape(count, -1, *value.shape[1:]), axis=0)


def gather_rows(value, axis):
    count = lax.axis_size(axis)
    return lax.all_to_all(jnp.tile(value, (count, 1)), axis, 0, 0, tiled=True)


def body(
    proposal_rows,
    norm_gain,
    query_weight,
    key_weight,
    value_weight,
    out_weight,
    context_keys,
    context_values,
    prefix_lengths,
    parents,
):
    other_rows = lax.ppermute(proposal_rows, "sec", [(0, 1), (1, 0)])
    first = lax.axis_index("sec") == 0
    gathered = jnp.where(
        first,
        jnp.concatenate([proposal_rows, other_rows], axis=0),
        jnp.concatenate([other_rows, proposal_rows], axis=0),
    )
    gathered_wide = gathered.astype(jnp.float32)
    total_rows = gathered.shape[0]
    squares = jnp.sum(gathered_wide * gathered_wide, axis=1)
    scaled = (gathered_wide * norm_gain.astype(jnp.float32)[None, :]).astype(jnp.bfloat16)
    query_width = query_weight.shape[1]
    head_size = key_weight.shape[2]
    groups = query_width // head_size
    joined = jnp.concatenate([query_weight, key_weight[:, 0, :], value_weight[:, 0, :]], axis=1)
    partial_value = jnp.dot(scaled, joined, preferred_element_type=jnp.float32)
    proj_width = partial_value.shape[1]
    lane = jnp.arange(128, dtype=jnp.int32)
    square_block = jnp.where(lane[None, :] == 0, squares[:, None], 0.0)
    packed = jnp.concatenate([partial_value, square_block], axis=1)
    reduced = reduce_rows(packed, "ctx")
    row_share = reduced.shape[0]
    inverse = lax.rsqrt(reduced[:, proj_width] / D + EPSILON)[:, None]
    settled = reduced[:, :proj_width] * inverse
    own_queries = settled[:, :query_width].astype(jnp.bfloat16)
    tree_keys = settled[:, query_width : query_width + head_size].astype(jnp.bfloat16)
    tree_vals = settled[:, query_width + head_size :].astype(jnp.bfloat16)
    queries = gather_rows(own_queries, "ctx")

    position = lax.axis_index("ctx")
    keys = context_keys[:, 0, :]
    vals = context_values[:, 0, :]
    span = keys.shape[0]
    factor = 1.0 / math.sqrt(head_size)
    lengths_rows = jnp.repeat(prefix_lengths, PROPOSALS)
    lengths_query = jnp.repeat(lengths_rows - position * span, groups)[:, None]
    tree_mask = jnp.repeat(
        ancestry_columns(parents, position * row_share, row_share).astype(jnp.bfloat16), groups, axis=0
    )
    summed, high, weight_sum = attend(
        queries.reshape(total_rows * groups, head_size), keys, vals, lengths_query,
        tree_keys, tree_vals, tree_mask, factor,
    )
    high = high.reshape(total_rows, groups)
    weight_sum = weight_sum.reshape(total_rows, groups)
    sum_hi = lax.reduce_precision(weight_sum, exponent_bits=8, mantissa_bits=7)
    sum_lo = weight_sum - sum_hi
    side_block = jnp.concatenate(
        [sum_hi, sum_lo, *split_three(high), jnp.zeros((total_rows, 128 - 5 * groups), jnp.float32)],
        axis=1,
    ).astype(jnp.bfloat16)
    packed_attn = jnp.concatenate([summed.reshape(total_rows, query_width), side_block], axis=1)
    count = lax.axis_size("ctx")
    moved = lax.all_to_all(packed_attn, "ctx", 0, 0, tiled=True).reshape(count, row_share, -1)
    moved = moved.astype(jnp.float32)
    shard_sums = moved[:, :, :query_width].reshape(count, row_share, groups, head_size)
    side = moved[:, :, query_width : query_width + 5 * groups].reshape(count, row_share, 5, groups)
    shard_weights = side[:, :, 0] + side[:, :, 1]
    shard_high = side[:, :, 2] + side[:, :, 3] + side[:, :, 4]
    top = jnp.max(shard_high, axis=0)
    shrink = jnp.exp(shard_high - top[None])
    total_sums = jnp.sum(shard_sums * shrink[:, :, :, None], axis=0)
    total_weights = jnp.sum(shard_weights * shrink, axis=0)
    own_attended = (
        (total_sums / total_weights[:, :, None]).reshape(row_share, query_width).astype(jnp.bfloat16)
    )
    attended = gather_rows(own_attended, "ctx")
    projected_out = jnp.dot(attended, out_weight, preferred_element_type=jnp.float32)
    return reduce_rows(projected_out, ("sec", "head")).astype(jnp.bfloat16)


def solution(mesh):
    placed = (
        P("sec", "ctx"),
        P("ctx"),
        P("ctx", ("sec", "head")),
        P("ctx", ("sec", "head"), None),
        P("ctx", ("sec", "head"), None),
        P(("sec", "head"), "ctx"),
        P("ctx", ("sec", "head"), None),
        P("ctx", ("sec", "head"), None),
        P(),
        P(),
    )
    return jax.shard_map(
        body, mesh=mesh, in_specs=placed, out_specs=P(("sec", "head"), "ctx"), check_vma=False
    )
```

```python
import math

import jax
import jax.numpy as jnp
from jax import lax
from jax.experimental import pallas as pl
from jax.experimental.pallas import tpu as pltpu
from jax.sharding import PartitionSpec as P

D = 8192
PROPOSALS = 16


NEGATIVE = -1e30
EPSILON = 1e-05


def ancestry_columns(parents, column_offset, column_amount):
    total = parents.shape[0]
    index = jnp.arange(total, dtype=jnp.int32)
    step = jnp.logical_or(parents[:, None] == index[None, :], index[:, None] == index[None, :])
    reach = step.astype(jnp.bfloat16)
    for _ in range(3):
        reach = (jnp.dot(reach, reach, preferred_element_type=jnp.float32) > 0).astype(jnp.bfloat16)
    columns = lax.dynamic_slice_in_dim(reach, column_offset, column_amount, 1)
    return jnp.dot(reach, columns, preferred_element_type=jnp.float32) > 0


def split_three(value):
    high = lax.reduce_precision(value, exponent_bits=8, mantissa_bits=7)
    rest = value - high
    middle = lax.reduce_precision(rest, exponent_bits=8, mantissa_bits=7)
    return high, middle, rest - middle


def attend_kernel(
    query_ref, key_ref, value_ref, bias_ref, tree_key_ref, tree_value_ref, tree_mask_ref,
    out_ref, side_ref, *, factor, groups, per_particle,
):
    keys = key_ref[...]
    vals = value_ref[...]
    tree_keys = tree_key_ref[...]
    tree_vals = tree_value_ref[...]
    bias = bias_ref[...]
    tree_visible = tree_mask_ref[...] > 0
    amount = query_ref.shape[0]
    head_size = keys.shape[1]
    span = keys.shape[0]
    particles = amount // per_particle
    lane = lax.broadcasted_iota(jnp.int32, side_ref.shape, 1)
    side = jnp.zeros(side_ref.shape, jnp.float32)
    for group in range(groups):
        query = query_ref[:, group * head_size : (group + 1) * head_size]
        scores = lax.dot_general(
            query, keys, (((1,), (1,)), ((), ())), preferred_element_type=jnp.float32
        ) * factor
        scores = (scores.reshape(particles, per_particle, span) + bias[:, None, :]).reshape(
            amount, span
        )
        tree_scores = lax.dot_general(
            query, tree_keys, (((1,), (1,)), ((), ())), preferred_element_type=jnp.float32
        ) * factor
        tree_scores = jnp.where(tree_visible, tree_scores, NEGATIVE)
        high = jnp.maximum(
            jnp.max(scores, axis=1, keepdims=True), jnp.max(tree_scores, axis=1, keepdims=True)
        )
        safe = jnp.where(high > 0.5 * NEGATIVE, high, 0.0)
        weights = jnp.exp(scores - safe)
        tree_weights = jnp.exp(tree_scores - safe)
        total = jnp.sum(weights, axis=1, keepdims=True) + jnp.sum(
            tree_weights, axis=1, keepdims=True
        )
        out_ref[:, group * head_size : (group + 1) * head_size] = (
            jnp.dot(weights.astype(jnp.bfloat16), vals, preferred_element_type=jnp.float32)
            + jnp.dot(
                tree_weights.astype(jnp.bfloat16), tree_vals, preferred_element_type=jnp.float32
            )
        ).astype(jnp.bfloat16)
        side = jnp.where(lane == group, total, side)
        side = jnp.where(lane == groups + group, high, side)
    out_ref[:, groups * head_size :] = jnp.zeros(
        (amount, out_ref.shape[1] - groups * head_size), jnp.bfloat16
    )
    side_ref[...] = side


def attend(queries, keys, vals, bias, tree_keys, tree_vals, tree_mask, factor, groups, per_particle,
           block=256):
    amount, width = queries.shape
    span, head_size = keys.shape
    tree_amount = tree_keys.shape[0]
    whole = lambda i: (0, 0)
    rows = lambda i: (i, 0)
    return pl.pallas_call(
        lambda *refs: attend_kernel(*refs, factor=factor, groups=groups, per_particle=per_particle),
        out_shape=(
            jax.ShapeDtypeStruct((amount, width + 128), jnp.bfloat16),
            jax.ShapeDtypeStruct((amount, 128), jnp.float32),
        ),
        grid=(amount // block,),
        in_specs=[
            pl.BlockSpec((block, width), rows),
            pl.BlockSpec((span, head_size), whole),
            pl.BlockSpec((span, head_size), whole),
            pl.BlockSpec((block // per_particle, span), rows),
            pl.BlockSpec((tree_amount, head_size), whole),
            pl.BlockSpec((tree_amount, head_size), whole),
            pl.BlockSpec((block, tree_amount), rows),
        ],
        out_specs=(
            pl.BlockSpec((block, width + 128), rows),
            pl.BlockSpec((block, 128), rows),
        ),
        compiler_params=pltpu.CompilerParams(dimension_semantics=("arbitrary",)),
    )(queries, keys, vals, bias, tree_keys, tree_vals, tree_mask)


def reduce_rows(value, axis):
    count = lax.axis_size(axis)
    moved = lax.all_to_all(value, axis, 0, 0, tiled=True)
    return jnp.sum(moved.reshape(count, -1, *value.shape[1:]), axis=0)


def gather_rows(value, axis):
    count = lax.axis_size(axis)
    return lax.all_to_all(jnp.tile(value, (count, 1)), axis, 0, 0, tiled=True)


def body(
    proposal_rows,
    norm_gain,
    query_weight,
    key_weight,
    value_weight,
    out_weight,
    context_keys,
    context_values,
    prefix_lengths,
    parents,
):
    other_rows = lax.ppermute(proposal_rows, "sec", [(0, 1), (1, 0)])
    first = lax.axis_index("sec") == 0
    gathered = jnp.where(
        first,
        jnp.concatenate([proposal_rows, other_rows], axis=0),
        jnp.concatenate([other_rows, proposal_rows], axis=0),
    )
    gathered_wide = gathered.astype(jnp.float32)
    total_rows = gathered.shape[0]
    squares = jnp.sum(gathered_wide * gathered_wide, axis=1)
    scaled = (gathered_wide * norm_gain.astype(jnp.float32)[None, :]).astype(jnp.bfloat16)
    query_width = query_weight.shape[1]
    head_size = key_weight.shape[2]
    groups = query_width // head_size
    joined = jnp.concatenate([query_weight, key_weight[:, 0, :], value_weight[:, 0, :]], axis=1)
    partial_value = jnp.dot(scaled, joined, preferred_element_type=jnp.float32)
    proj_width = partial_value.shape[1]
    lane = jnp.arange(128, dtype=jnp.int32)
    square_block = jnp.where(lane[None, :] == 0, squares[:, None], 0.0)
    packed = jnp.concatenate([partial_value, square_block], axis=1)
    reduced = reduce_rows(packed, "ctx")
    row_share = reduced.shape[0]
    inverse = lax.rsqrt(reduced[:, proj_width] / D + EPSILON)[:, None]
    settled = reduced[:, :proj_width] * inverse
    own_queries = settled[:, :query_width].astype(jnp.bfloat16)
    tree_keys = settled[:, query_width : query_width + head_size].astype(jnp.bfloat16)
    tree_vals = settled[:, query_width + head_size :].astype(jnp.bfloat16)
    queries = gather_rows(own_queries, "ctx")

    position = lax.axis_index("ctx")
    keys = context_keys[:, 0, :]
    vals = context_values[:, 0, :]
    span = keys.shape[0]
    factor = 1.0 / math.sqrt(head_size)
    positions = position * span + jnp.arange(span, dtype=jnp.int32)
    bias = jnp.where(positions[None, :] < prefix_lengths[:, None], 0.0, NEGATIVE)
    tree_mask = ancestry_columns(parents, position * row_share, row_share).astype(jnp.bfloat16)
    packed_attn, side = attend(
        queries, keys, vals, bias, tree_keys, tree_vals, tree_mask, factor, groups, PROPOSALS
    )
    weight_sum = side[:, :groups]
    high = side[:, groups : 2 * groups]
    sum_hi = lax.reduce_precision(weight_sum, exponent_bits=8, mantissa_bits=7)
    sum_lo = weight_sum - sum_hi
    side_block = jnp.concatenate(
        [sum_hi, sum_lo, *split_three(high), jnp.zeros((total_rows, 128 - 5 * groups), jnp.float32)],
        axis=1,
    ).astype(jnp.bfloat16)
    packed_attn = lax.dynamic_update_slice(packed_attn, side_block, (0, query_width))
    count = lax.axis_size("ctx")
    moved = lax.all_to_all(packed_attn, "ctx", 0, 0, tiled=True).reshape(count, row_share, -1)
    moved = moved.astype(jnp.float32)
    shard_sums = moved[:, :, :query_width].reshape(count, row_share, groups, head_size)
    side = moved[:, :, query_width : query_width + 5 * groups].reshape(count, row_share, 5, groups)
    shard_weights = side[:, :, 0] + side[:, :, 1]
    shard_high = side[:, :, 2] + side[:, :, 3] + side[:, :, 4]
    top = jnp.max(shard_high, axis=0)
    shrink = jnp.exp(shard_high - top[None])
    total_sums = jnp.sum(shard_sums * shrink[:, :, :, None], axis=0)
    total_weights = jnp.sum(shard_weights * shrink, axis=0)
    own_attended = (
        (total_sums / total_weights[:, :, None]).reshape(row_share, query_width).astype(jnp.bfloat16)
    )
    attended = gather_rows(own_attended, "ctx")
    projected_out = jnp.dot(attended, out_weight, preferred_element_type=jnp.float32)
    return reduce_rows(projected_out, ("sec", "head")).astype(jnp.bfloat16)


def solution(mesh):
    placed = (
        P("sec", "ctx"),
        P("ctx"),
        P("ctx", ("sec", "head")),
        P("ctx", ("sec", "head"), None),
        P("ctx", ("sec", "head"), None),
        P(("sec", "head"), "ctx"),
        P("ctx", ("sec", "head"), None),
        P("ctx", ("sec", "head"), None),
        P(),
        P(),
    )
    return jax.shard_map(
        body, mesh=mesh, in_specs=placed, out_specs=P(("sec", "head"), "ctx"), check_vma=False
    )
```
